512 devices in a mesh: pipe: 8 (over z_hi, y), expert: 64 (over z_lo, x, core).
Axes of the slice: x: 4, y: 4, z: 16 (z_hi: 2, z_lo: 8; z = z_hi * 8 + z_lo), core: 2. Of those that a mesh axis runs over, the one named last changes fastest.
Arguments:
- tokens: bfloat16 [65536, 2048], P(('pipe', 'expert')), may hold values from -6 to 6
- cotangent: bfloat16 [65536, 2048], P(('pipe', 'expert')), may hold values from -6 to 6
- expert_ids: int32 [65536, 8], P(('pipe', 'expert')), may hold values from 0 to 127, all different within a row
- gates: float32 [65536, 8], P(('pipe', 'expert')), may hold values from 0.05 to 0.5
- w_gate: bfloat16 [8, 2048, 12288], P('pipe', None, 'expert'), as said below
- w_up: bfloat16 [8, 2048, 12288], P('pipe', None, 'expert'), as said below
- w_down: bfloat16 [8, 12288, 2048], P('pipe', 'expert'), as said below
Outputs:
- mixed_out: bfloat16 [65536, 2048], P(('pipe', 'expert'))
- token_grad: bfloat16 [65536, 2048], P(('pipe', 'expert'))
- gate_grad: float32 [65536, 8], P(('pipe', 'expert'))
- down_grad: bfloat16 [8, 12288, 1024], P('pipe', 'expert')
The draws below stay inside these ranges and needn't reach their ends.
Inputs may be any that keep to these rules, and one draw needn't show every extreme that they name: `expert_ids`: each row names 8 different experts. `w_gate`: the blocks of pipe index p and 7 - p are equal. `w_up`: the blocks of pipe index p and 7 - p are equal. `w_down`: the blocks of pipe index p and 7 - p are equal.
All inputs are finite; a program needn't handle non-finite values.
Results may differ from the reference program's by a relative error of at most 0.0065.
Values may be sent and summed in bfloat16 or wider, within the bound.
No kernel may reach another device: no remote copies, remote signals or barrier semaphores. Data moves between devices by JAX's collectives and lax.ppermute only.
A program may use at most 64 MiB of HBM per device.

```python
import math
import jax
import jax.numpy as jnp
from jax import lax

D = 2048
EXPERTS = 128
TOPK = 8
FFW = 768
WS = 4
FS = 192
EW = 16
TOK_DEV = 128
CAP = 5
TOKENS = 65536
N_PIPE = 8
N_EXPERT = 64


def mirrored(key, rows, cols, fan_in):
    half_set = jnp.clip(jax.random.normal(key, (N_PIPE // 2, rows, cols), jnp.float32), -6.0, 6.0) * fan_in ** (-0.5)
    return jnp.concatenate([half_set, half_set[::-1]], axis=0)


def draw_w_gate(key, part):
    return mirrored(jax.random.fold_in(key, 101), D, EW * FFW, D).astype(jnp.bfloat16)


def draw_w_up(key, part):
    return mirrored(jax.random.fold_in(key, 202), D, EW * FFW, D).astype(jnp.bfloat16)


def draw_w_down(key, part):
    return mirrored(jax.random.fold_in(key, 303), EW * FFW, D, FFW).astype(jnp.bfloat16)


def block_levels(key, shape, split, least, top_value):
    def one(position, shards_of):
        draws = jax.random.uniform(jax.random.fold_in(jax.random.fold_in(key, 6), position), (shards_of,), jnp.float32, least / len(split), top_value / len(split))
        return jnp.repeat(jnp.exp(draws), shape[position] // shards_of).reshape((-1,) + (1,) * (len(shape) - position - 1))

    gain = one(*split[0])
    for cut in split[1:]:
        gain = gain * one(*cut)
    return gain


def picks_of(own_key, rows, count, top, lift):
    sequence = jax.random.permutation(jax.random.fold_in(own_key, 1), count)
    pull = sequence
    for power in range(3):
        pull = pull * pull // count
    pull = pull * lift // count
    tickets = jax.random.randint(jax.random.fold_in(own_key, 2), (rows, count), 0, 4096) + pull
    sure = jax.random.permutation(jax.random.fold_in(own_key, 3), rows)[jnp.arange(count) % rows]
    tickets = jnp.where(jnp.arange(rows)[:, None] == sure[None, :], 1 << 14, tickets)
    score = tickets * count + jnp.arange(count)
    return lax.top_k(score.astype(jnp.int32), top)[1].astype(jnp.int32)


def centred(rng, dims, width, bound, pieces=(), held_as=jnp.bfloat16):
    array = jax.random.normal(rng, dims, jnp.float32) * width
    if len(pieces) > 0:
        array = block_levels(rng, dims, pieces, -0.22, 0.18) * array
    return jnp.clip(array, min=-bound, max=bound).astype(held_as)


def setup_inputs(seed: int = 0) -> dict:
    keys = jax.random.split(jax.random.key(seed), 8)
    tokens = centred(keys[0], (TOKENS, D), 1.0, 6.0, ((0, 512),))
    cotangent = centred(keys[1], (TOKENS, D), 1.0, 6.0, ((0, 512),))
    expert_ids = picks_of(keys[2], TOKENS, EXPERTS, TOPK, 1024)
    gates = jnp.clip(jnp.exp(math.log(0.5) - 2.3025851 * jax.random.uniform(keys[3], (TOKENS, TOPK), jnp.float32) ** block_levels(keys[3], (TOKENS, TOPK), ((0, 512),), -0.2, 0.2)), 0.05, 0.5)
    w_gate = draw_w_gate(jax.random.fold_in(keys[7], 71), 0)
    w_up = draw_w_up(jax.random.fold_in(keys[7], 71), 0)
    w_down = draw_w_down(jax.random.fold_in(keys[7], 71), 0)
    return dict(tokens=tokens, cotangent=cotangent, expert_ids=expert_ids, gates=gates, w_gate=w_gate, w_up=w_up, w_down=w_down)


def silu_parts(preact):
    sigmoid_val = jax.nn.sigmoid(preact)
    return preact * sigmoid_val, sigmoid_val * (1.0 + preact * (1.0 - sigmoid_val))


def rounded_f32(values):
    return lax.optimization_barrier(values.astype(jnp.bfloat16)).astype(jnp.float32)


def section_layer(rows_in, rows_cot, ids_here, gates_here, gate_mat, up_mat, down_mat):
    tok_rows = rows_in.shape[0]
    row_bound = N_EXPERT * CAP
    padded_in = jnp.concatenate([rows_in, jnp.zeros((1, D), rows_in.dtype)])
    padded_cot = jnp.concatenate([rows_cot, jnp.zeros((1, D), rows_cot.dtype)])
    highest = lax.Precision.HIGHEST

    def one_expert(expert_no):
        gate_cols = lax.dynamic_slice_in_dim(gate_mat, expert_no * FFW, FFW, 1)
        up_cols = lax.dynamic_slice_in_dim(up_mat, expert_no * FFW, FFW, 1)
        down_rows = lax.dynamic_slice_in_dim(down_mat, expert_no * FFW, FFW, 0)
        named = (ids_here == expert_no).astype(jnp.int32).reshape(N_EXPERT, TOK_DEV * TOPK)
        before = jnp.cumsum(named, axis=1) - named
        matches = ((named == 1) & (before < CAP)).reshape(tok_rows, TOPK)
        row_gate = jnp.sum(jnp.where(matches, gates_here, 0.0), axis=1)
        gate_padded = jnp.concatenate([row_gate, jnp.zeros((1,), row_gate.dtype)])
        chosen = jnp.nonzero(jnp.any(matches, axis=1), size=row_bound, fill_value=tok_rows)[0].astype(jnp.int32)
        inputs = padded_in[chosen]
        cot_rows = padded_cot[chosen].astype(jnp.float32)
        slot_gate = gate_padded[chosen]
        scaled = (slot_gate[:, None] * cot_rows).astype(jnp.bfloat16)
        gate_pre = jnp.dot(inputs, gate_cols, preferred_element_type=jnp.float32)
        up_pre = jnp.dot(inputs, up_cols, preferred_element_type=jnp.float32)
        activated, slope_val = silu_parts(gate_pre)
        hidden = (activated * up_pre).astype(jnp.bfloat16)
        hidden_groups = hidden.astype(jnp.float32).reshape(row_bound, WS, FS)
        down_groups = down_rows.astype(jnp.float32).reshape(WS, FS, D)
        group_out = jnp.einsum("rgf,gfd->grd", hidden_groups, down_groups, precision=highest)
        expert_out = jnp.sum(rounded_f32(group_out), axis=0)
        hidden_grad = jnp.dot(scaled, down_rows.T, preferred_element_type=jnp.float32)
        grad_gate = (hidden_grad * up_pre * slope_val).astype(jnp.bfloat16)
        grad_up = (hidden_grad * activated).astype(jnp.bfloat16)
        gate_groups = gate_cols.astype(jnp.float32).reshape(D, WS, FS)
        up_groups = up_cols.astype(jnp.float32).reshape(D, WS, FS)
        back_gate = jnp.einsum("rgf,dgf->grd", grad_gate.astype(jnp.float32).reshape(row_bound, WS, FS), gate_groups, precision=highest)
        back_up = jnp.einsum("rgf,dgf->grd", grad_up.astype(jnp.float32).reshape(row_bound, WS, FS), up_groups, precision=highest)
        token_part = jnp.sum(rounded_f32(back_gate + back_up), axis=0)
        down_part = jnp.dot(hidden.T, scaled, preferred_element_type=jnp.float32)
        slot_value = jnp.sum(cot_rows * expert_out, axis=1)
        match_padded = jnp.concatenate([matches, jnp.zeros((1, TOPK), jnp.bool_)])
        gate_part = slot_value[:, None] * match_padded[chosen].astype(jnp.float32)
        return chosen, slot_gate, expert_out, token_part, down_part, gate_part

    chosen, slot_gate, expert_out, token_part, down_part, gate_part = lax.map(one_expert, jnp.arange(EW, dtype=jnp.int32))
    flat_rows = chosen.reshape(-1)
    mixed_sum = jnp.zeros((tok_rows + 1, D), jnp.float32).at[flat_rows].add((slot_gate[:, :, None] * expert_out).reshape(-1, D))
    token_sum = jnp.zeros((tok_rows + 1, D), jnp.float32).at[flat_rows].add(token_part.reshape(-1, D))
    gate_sum = jnp.zeros((tok_rows + 1, TOPK), jnp.float32).at[flat_rows].add(gate_part.reshape(-1, TOPK))
    return (mixed_sum[:tok_rows].astype(jnp.bfloat16), token_sum[:tok_rows].astype(jnp.bfloat16),
            gate_sum[:tok_rows], down_part.reshape(EW * FFW, D))


def reference(tokens, cotangent, expert_ids, gates, w_gate, w_up, w_down):
    per_section = N_EXPERT * TOK_DEV
    mixed_list, token_list, gate_list, local_list = [], [], [], []
    for section_no in range(N_PIPE):
        first_row = section_no * per_section
        results = section_layer(tokens[first_row:first_row + per_section], cotangent[first_row:first_row + per_section],
                              expert_ids[first_row:first_row + per_section], gates[first_row:first_row + per_section],
                              w_gate[section_no], w_up[section_no], w_down[section_no])
        mixed_list.append(results[0])
        token_list.append(results[1])
        gate_list.append(results[2])
        local_list.append(results[3])
    local_down = rounded_f32(jnp.stack(local_list))
    summed = local_down + local_down[::-1]
    half_width = D // 2
    halves = []
    for section_no in range(N_PIPE):
        offset = half_width if section_no >= N_PIPE // 2 else 0
        halves.append(summed[section_no, :, offset:offset + half_width])
    down_grad = jnp.stack(halves).astype(jnp.bfloat16)
    return (jnp.concatenate(mixed_list), jnp.concatenate(token_list), jnp.concatenate(gate_list), down_grad)
```

```python
import jax
import jax.numpy as jnp
from jax import lax
from jax.sharding import Mesh, PartitionSpec as P

WS = 4


def from_partner(block, axis, stride):
    count = lax.axis_size(axis)
    route = []
    for low in range(count):
        high = low | 1 << stride
        if high != low and high < count:
            route += [(low, high), (high, low)]
    return lax.ppermute(block, axis, route)


def silu_parts(preact):
    sigmoid_val = jax.nn.sigmoid(preact)
    return (preact * sigmoid_val, sigmoid_val * (1.0 + preact * (1.0 - sigmoid_val)))


def expert_rows(inputs, scaled, gate_cols, up_cols, down_rows):
    transposed = (((1,), (1,)), ((), ()))
    gate_pre = jnp.dot(inputs, gate_cols, preferred_element_type=jnp.float32)
    up_pre = jnp.dot(inputs, up_cols, preferred_element_type=jnp.float32)
    activated, slope_val = silu_parts(gate_pre)
    hidden = (activated * up_pre).astype(jnp.bfloat16)
    group_out = jnp.dot(hidden, down_rows, preferred_element_type=jnp.float32).astype(jnp.bfloat16)
    hidden_grad = lax.dot_general(scaled, down_rows, transposed, preferred_element_type=jnp.float32)
    grad_gate = (hidden_grad * up_pre * slope_val).astype(jnp.bfloat16)
    grad_up = (hidden_grad * activated).astype(jnp.bfloat16)
    back_gate = lax.dot_general(
        grad_gate, gate_cols, transposed, preferred_element_type=jnp.float32
    )
    back_up = lax.dot_general(grad_up, up_cols, transposed, preferred_element_type=jnp.float32)
    group_grad = (back_gate + back_up).astype(jnp.bfloat16)
    return (hidden, group_out, group_grad)


def split_half(stacked, upper_half):
    half_width = stacked.shape[-1] // 2
    lower_part = stacked[..., :half_width]
    upper_part = stacked[..., half_width:]
    kept_half = jnp.where(upper_half, upper_part, lower_part)
    sent_half = jnp.where(upper_half, lower_part, upper_part)
    return (kept_half, sent_half)


def body(tokens, cotangent, expert_ids, gates, w_gate, w_up, w_down):
    highest = lax.Precision.HIGHEST
    tok_count, model_width = tokens.shape
    chosen_count = expert_ids.shape[1]
    experts_here = lax.axis_size("eg")
    shards = lax.axis_size("es")
    capacity = tok_count // 24
    slot_count = experts_here * capacity
    flat_ids = expert_ids.reshape(-1)
    window_ids = jnp.arange(experts_here, dtype=jnp.int32)
    onehot = (flat_ids[:, None] == window_ids[None, :]).astype(jnp.int32)
    earlier = jnp.cumsum(onehot, axis=0) - onehot
    slot_rank = jnp.sum(earlier * onehot, axis=1)
    in_window = (flat_ids < experts_here) & (slot_rank < capacity)
    target_slot = jnp.where(in_window, flat_ids * capacity + slot_rank, slot_count)
    slot_numbers = jnp.arange(slot_count, dtype=jnp.int32)
    pick_pair = (target_slot[None, :] == slot_numbers[:, None]).astype(jnp.float32)
    pick_token = pick_pair.reshape(slot_count, tok_count, chosen_count).sum(axis=2)
    slot_gate = jnp.dot(pick_pair, gates.reshape(-1), precision=highest)
    pick_narrow = pick_token.astype(jnp.bfloat16)
    slot_rows = jnp.dot(pick_narrow, tokens, preferred_element_type=jnp.float32).astype(
        jnp.bfloat16
    )
    slot_cot = jnp.dot(pick_narrow, cotangent, preferred_element_type=jnp.float32)
    slot_scaled = (slot_gate[:, None] * slot_cot).astype(jnp.bfloat16)

    payload = jnp.concatenate([slot_rows, slot_scaled], axis=1).reshape(experts_here, -1)
    arrived = lax.all_to_all(payload, "eg", 0, 0, tiled=True)
    copies = jnp.broadcast_to(arrived[None], (shards,) + arrived.shape).reshape(
        shards * experts_here, -1
    )
    gathered = lax.all_to_all(copies, "es", 0, 0, tiled=True)
    gathered = gathered.reshape(shards * experts_here * capacity, 2 * model_width)
    inputs = gathered[:, :model_width]
    scaled = gathered[:, model_width:]
    hidden, group_out, group_grad = expert_rows(
        inputs, scaled, w_gate[0], w_up[0], w_down[0]
    )

    parts = jnp.concatenate([group_out, group_grad], axis=1).reshape(shards, -1)
    parts = lax.all_to_all(parts, "es", 0, 0, tiled=True)
    summed = parts.reshape(shards, -1).astype(jnp.float32).sum(axis=0)
    summed = summed.astype(jnp.bfloat16).reshape(experts_here, -1)
    returned = lax.all_to_all(summed, "eg", 0, 0, tiled=True)
    returned = returned.reshape(slot_count, 2 * model_width).astype(jnp.float32)
    expert_out = returned[:, :model_width]
    grad_terms = returned[:, model_width:]

    weighted = slot_gate[:, None] * expert_out
    mixed_out = jnp.dot(pick_token.T, weighted, precision=highest).astype(jnp.bfloat16)
    slot_value = jnp.sum(slot_cot * expert_out, axis=1)
    gate_grad = jnp.dot(slot_value, pick_pair, precision=highest).reshape(tok_count, chosen_count)
    token_grad = jnp.dot(pick_token.T, grad_terms, precision=highest).astype(jnp.bfloat16)
    local_down = lax.dot_general(
        hidden,
        scaled,
        (((0,), (0,)), ((), ())),
        preferred_element_type=jnp.float32,
    ).astype(jnp.bfloat16)
    sections = lax.axis_size("pipe")
    section_pos = lax.axis_index("pipe")
    kept_half, sent_half = split_half(local_down, section_pos >= sections // 2)
    mirror = [(p, sections - 1 - p) for p in range(sections)]
    partner_part = lax.ppermute(sent_half, "pipe", mirror).astype(jnp.float32)
    down_grad = (kept_half.astype(jnp.float32) + partner_part).astype(jnp.bfloat16)[None]
    return (mixed_out, token_grad, gate_grad, down_grad)


def solution(mesh):
    experts = mesh.shape["expert"]
    split = Mesh(
        mesh.devices.reshape(mesh.shape["pipe"], experts // WS, WS), ("pipe", "eg", "es")
    )
    rows = P(("pipe", "eg", "es"), None)
    placed = (
        rows,
        rows,
        rows,
        rows,
        P("pipe", None, ("eg", "es")),
        P("pipe", None, ("eg", "es")),
        P("pipe", ("eg", "es"), None),
    )
    return jax.shard_map(
        body,
        mesh=split,
        in_specs=placed,
        out_specs=(rows, rows, rows, P("pipe", ("eg", "es"), None)),
        check_vma=False,
    )
```

```python
import jax
import jax.numpy as jnp
from jax import lax
from jax.sharding import Mesh, PartitionSpec as P

WS = 4


def from_partner(block, axis, stride):
    count = lax.axis_size(axis)
    route = []
    for low in range(count):
        high = low | 1 << stride
        if high != low and high < count:
            route += [(low, high), (high, low)]
    return lax.ppermute(block, axis, route)


def silu_parts(preact):
    sigmoid_val = jax.nn.sigmoid(preact)
    return (preact * sigmoid_val, sigmoid_val * (1.0 + preact * (1.0 - sigmoid_val)))


def expert_rows(inputs, scaled, gate_cols, up_cols, down_rows):
    transposed = (((1,), (1,)), ((), ()))
    gate_pre = jnp.dot(inputs, gate_cols, preferred_element_type=jnp.float32)
    up_pre = jnp.dot(inputs, up_cols, preferred_element_type=jnp.float32)
    activated, slope_val = silu_parts(gate_pre)
    hidden = (activated * up_pre).astype(jnp.bfloat16)
    group_out = jnp.dot(hidden, down_rows, preferred_element_type=jnp.float32).astype(jnp.bfloat16)
    hidden_grad = lax.dot_general(scaled, down_rows, transposed, preferred_element_type=jnp.float32)
    grad_gate = (hidden_grad * up_pre * slope_val).astype(jnp.bfloat16)
    grad_up = (hidden_grad * activated).astype(jnp.bfloat16)
    back_gate = lax.dot_general(
        grad_gate, gate_cols, transposed, preferred_element_type=jnp.float32
    )
    back_up = lax.dot_general(grad_up, up_cols, transposed, preferred_element_type=jnp.float32)
    group_grad = (back_gate + back_up).astype(jnp.bfloat16)
    return (hidden, group_out, group_grad)


def split_half(stacked, upper_half):
    half_width = stacked.shape[-1] // 2
    lower_part = stacked[..., :half_width]
    upper_part = stacked[..., half_width:]
    kept_half = jnp.where(upper_half, upper_part, lower_part)
    sent_half = jnp.where(upper_half, lower_part, upper_part)
    return (kept_half, sent_half)


def body(tokens, cotangent, expert_ids, gates, w_gate, w_up, w_down):
    highest = lax.Precision.HIGHEST
    tok_count, model_width = tokens.shape
    chosen_count = expert_ids.shape[1]
    experts_here = lax.axis_size("eg")
    shards = lax.axis_size("es")
    capacity = tok_count // 24
    slot_count = experts_here * capacity
    flat_ids = expert_ids.reshape(-1)
    window_ids = jnp.arange(experts_here, dtype=jnp.int32)
    onehot = (flat_ids[:, None] == window_ids[None, :]).astype(jnp.int32)
    earlier = jnp.cumsum(onehot, axis=0) - onehot
    slot_rank = jnp.sum(earlier * onehot, axis=1)
    in_window = (flat_ids < experts_here) & (slot_rank < capacity)
    target_slot = jnp.where(in_window, flat_ids * capacity + slot_rank, slot_count)
    slot_numbers = jnp.arange(slot_count, dtype=jnp.int32)
    pick_pair = (target_slot[None, :] == slot_numbers[:, None]).astype(jnp.float32)
    pick_token = pick_pair.reshape(slot_count, tok_count, chosen_count).sum(axis=2)
    slot_gate = jnp.dot(pick_pair, gates.reshape(-1), precision=highest)
    pick_narrow = pick_token.astype(jnp.bfloat16)
    slot_rows = jnp.dot(pick_narrow, tokens, preferred_element_type=jnp.float32).astype(
        jnp.bfloat16
    )
    slot_cot = jnp.dot(pick_narrow, cotangent, preferred_element_type=jnp.float32)
    slot_scaled = (slot_gate[:, None] * slot_cot).astype(jnp.bfloat16)

    tile_rows = 16
    payload = jnp.concatenate([slot_rows, slot_scaled], axis=1).reshape(
        experts_here, tile_rows, -1
    )
    arrived = lax.all_to_all(payload, "eg", 0, 0, tiled=True)
    copies = jnp.broadcast_to(arrived[None], (shards,) + arrived.shape).reshape(
        (shards * experts_here,) + arrived.shape[1:]
    )
    gathered = lax.all_to_all(copies, "es", 0, 0, tiled=True)
    gathered = gathered.reshape(shards * experts_here * capacity, 2 * model_width)
    inputs = gathered[:, :model_width]
    scaled = gathered[:, model_width:]
    hidden, group_out, group_grad = expert_rows(
        inputs, scaled, w_gate[0], w_up[0], w_down[0]
    )

    parts = jnp.concatenate([group_out, group_grad], axis=1).reshape(shards, slot_count, -1)
    parts = lax.all_to_all(parts, "es", 0, 0, tiled=True)
    summed = parts.astype(jnp.float32).sum(axis=0)
    summed = summed.astype(jnp.bfloat16).reshape(experts_here, tile_rows, -1)
    returned = lax.all_to_all(summed, "eg", 0, 0, tiled=True)
    returned = returned.reshape(slot_count, 2 * model_width).astype(jnp.float32)
    expert_out = returned[:, :model_width]
    grad_terms = returned[:, model_width:]

    weighted = slot_gate[:, None] * expert_out
    mixed_out = jnp.dot(pick_token.T, weighted, precision=highest).astype(jnp.bfloat16)
    slot_value = jnp.sum(slot_cot * expert_out, axis=1)
    gate_grad = jnp.dot(slot_value, pick_pair, precision=highest).reshape(tok_count, chosen_count)
    token_grad = jnp.dot(pick_token.T, grad_terms, precision=highest).astype(jnp.bfloat16)
    local_down = lax.dot_general(
        hidden,
        scaled,
        (((0,), (0,)), ((), ())),
        preferred_element_type=jnp.float32,
    ).astype(jnp.bfloat16)
    sections = lax.axis_size("pipe")
    section_pos = lax.axis_index("pipe")
    kept_half, sent_half = split_half(local_down, section_pos >= sections // 2)
    mirror = [(p, sections - 1 - p) for p in range(sections)]
    partner_part = lax.ppermute(sent_half, "pipe", mirror).astype(jnp.float32)
    down_grad = (kept_half.astype(jnp.float32) + partner_part).astype(jnp.bfloat16)[None]
    return (mixed_out, token_grad, gate_grad, down_grad)


def solution(mesh):
    experts = mesh.shape["expert"]
    split = Mesh(
        mesh.devices.reshape(mesh.shape["pipe"], experts // WS, WS), ("pipe", "eg", "es")
    )
    rows = P(("pipe", "eg", "es"), None)
    placed = (
        rows,
        rows,
        rows,
        rows,
        P("pipe", None, ("eg", "es")),
        P("pipe", None, ("eg", "es")),
        P("pipe", ("eg", "es"), None),
    )
    return jax.shard_map(
        body,
        mesh=split,
        in_specs=placed,
        out_specs=(rows, rows, rows, P("pipe", ("eg", "es"), None)),
        check_vma=False,
    )
```

```python
import jax
import jax.numpy as jnp
from jax import lax
from jax.sharding import Mesh, PartitionSpec as P


WS = 4


def silu_parts(preact):
    sigmoid_val = jax.nn.sigmoid(preact)
    return (preact * sigmoid_val, sigmoid_val * (1.0 + preact * (1.0 - sigmoid_val)))


def expert_rows(inputs, scaled, gate_cols, up_cols, down_rows):
    transposed = (((1,), (1,)), ((), ()))
    gate_pre = jnp.dot(inputs, gate_cols, preferred_element_type=jnp.float32)
    up_pre = jnp.dot(inputs, up_cols, preferred_element_type=jnp.float32)
    activated, slope_val = silu_parts(gate_pre)
    hidden = (activated * up_pre).astype(jnp.bfloat16)
    group_out = jnp.dot(hidden, down_rows, preferred_element_type=jnp.float32).astype(jnp.bfloat16)
    hidden_grad = lax.dot_general(scaled, down_rows, transposed, preferred_element_type=jnp.float32)
    grad_gate = (hidden_grad * up_pre * slope_val).astype(jnp.bfloat16)
    grad_up = (hidden_grad * activated).astype(jnp.bfloat16)
    back_gate = lax.dot_general(
        grad_gate, gate_cols, transposed, preferred_element_type=jnp.float32
    )
    back_up = lax.dot_general(grad_up, up_cols, transposed, preferred_element_type=jnp.float32)
    group_grad = (back_gate + back_up).astype(jnp.bfloat16)
    return (hidden, group_out, group_grad)


def split_half(stacked, upper_half):
    half_width = stacked.shape[-1] // 2
    lower_part = stacked[..., :half_width]
    upper_part = stacked[..., half_width:]
    kept_half = jnp.where(upper_half, upper_part, lower_part)
    sent_half = jnp.where(upper_half, lower_part, upper_part)
    return (kept_half, sent_half)


def layer(tokens, cotangent, expert_ids, gates, w_gate, w_up, w_down):
    highest = lax.Precision.HIGHEST
    tok_count, model_width = tokens.shape
    chosen_count = expert_ids.shape[1]
    experts_here = lax.axis_size("eg")
    shards = lax.axis_size("es")
    capacity = tok_count // 24
    slot_count = experts_here * capacity
    flat_ids = expert_ids.reshape(-1)
    window_ids = jnp.arange(experts_here, dtype=jnp.int32)
    onehot = (flat_ids[:, None] == window_ids[None, :]).astype(jnp.int32)
    earlier = jnp.cumsum(onehot, axis=0) - onehot
    slot_rank = jnp.sum(earlier * onehot, axis=1)
    in_window = (flat_ids < experts_here) & (slot_rank < capacity)
    target_slot = jnp.where(in_window, flat_ids * capacity + slot_rank, slot_count)
    slot_numbers = jnp.arange(slot_count, dtype=jnp.int32)
    pick_pair = (target_slot[None, :] == slot_numbers[:, None]).astype(jnp.float32)
    pick_token = pick_pair.reshape(slot_count, tok_count, chosen_count).sum(axis=2)
    slot_gate = jnp.dot(pick_pair, gates.reshape(-1), precision=highest)
    pick_narrow = pick_token.astype(jnp.bfloat16)
    slot_rows = jnp.dot(pick_narrow, tokens, preferred_element_type=jnp.float32).astype(
        jnp.bfloat16
    )
    slot_cot = jnp.dot(pick_narrow, cotangent, preferred_element_type=jnp.float32)
    slot_scaled = (slot_gate[:, None] * slot_cot).astype(jnp.bfloat16)

    tile_rows = 16
    payload = jnp.concatenate([slot_rows, slot_scaled], axis=1).reshape(
        experts_here, tile_rows, -1
    )
    arrived = lax.all_to_all(payload, "eg", 0, 0, tiled=True)
    copies = jnp.broadcast_to(arrived[None], (shards,) + arrived.shape).reshape(
        (shards * experts_here,) + arrived.shape[1:]
    )
    gathered = lax.all_to_all(copies, "es", 0, 0, tiled=True)
    gathered = gathered.reshape(shards * experts_here * capacity, 2 * model_width)
    inputs = gathered[:, :model_width]
    scaled = gathered[:, model_width:]
    hidden, group_out, group_grad = expert_rows(
        inputs, scaled, w_gate[0], w_up[0], w_down[0]
    )

    parts = jnp.concatenate([group_out, group_grad], axis=1).reshape(shards, slot_count, -1)
    parts = lax.all_to_all(parts, "es", 0, 0, tiled=True)
    summed = parts.astype(jnp.float32).sum(axis=0)
    summed = summed.astype(jnp.bfloat16).reshape(experts_here, tile_rows, -1)
    returned = lax.all_to_all(summed, "eg", 0, 0, tiled=True)
    returned = returned.reshape(slot_count, 2 * model_width).astype(jnp.float32)
    expert_out = returned[:, :model_width]
    grad_terms = returned[:, model_width:]

    weighted = slot_gate[:, None] * expert_out
    mixed_out = jnp.dot(pick_token.T, weighted, precision=highest).astype(jnp.bfloat16)
    slot_value = jnp.sum(slot_cot * expert_out, axis=1)
    gate_grad = jnp.dot(slot_value, pick_pair, precision=highest).reshape(tok_count, chosen_count)
    token_grad = jnp.dot(pick_token.T, grad_terms, precision=highest).astype(jnp.bfloat16)
    local_down = lax.dot_general(
        hidden,
        scaled,
        (((0,), (0,)), ((), ())),
        preferred_element_type=jnp.float32,
    ).astype(jnp.bfloat16)
    sections = lax.axis_size("pipe")
    section_pos = lax.axis_index("pipe")
    kept_half, sent_half = split_half(local_down, section_pos >= sections // 2)
    mirror = [(p, sections - 1 - p) for p in range(sections)]
    partner_part = lax.ppermute(sent_half, "pipe", mirror)
    partner_part = partner_part.astype(jnp.float32)
    down_grad = (kept_half.astype(jnp.float32) + partner_part).astype(jnp.bfloat16)[None]
    return (mixed_out, token_grad, gate_grad, down_grad)


def solution(mesh):
    experts = mesh.shape["expert"]
    split = Mesh(
        mesh.devices.reshape(mesh.shape["pipe"], experts // WS, WS), ("pipe", "eg", "es")
    )
    rows = P(("pipe", "eg", "es"), None)
    placed = (
        rows,
        rows,
        rows,
        rows,
        P("pipe", None, ("eg", "es")),
        P("pipe", None, ("eg", "es")),
        P("pipe", ("eg", "es"), None),
    )
    return jax.shard_map(
        layer,
        mesh=split,
        in_specs=placed,
        out_specs=(rows, rows, rows, P("pipe", ("eg", "es"), None)),
        check_vma=False,
    )
```

```python
import jax
import jax.numpy as jnp
from jax import lax
from jax.sharding import Mesh, PartitionSpec as P


WS = 4


def silu_parts(preact):
    sigmoid_val = jax.nn.sigmoid(preact)
    return (preact * sigmoid_val, sigmoid_val * (1.0 + preact * (1.0 - sigmoid_val)))


def expert_rows(inputs, scaled, gate_cols, up_cols, down_rows):
    transposed = (((1,), (1,)), ((), ()))
    gate_pre = jnp.dot(inputs, gate_cols, preferred_element_type=jnp.float32)
    up_pre = jnp.dot(inputs, up_cols, preferred_element_type=jnp.float32)
    activated, slope_val = silu_parts(gate_pre)
    hidden = (activated * up_pre).astype(jnp.bfloat16)
    group_out = jnp.dot(hidden, down_rows, preferred_element_type=jnp.float32).astype(jnp.bfloat16)
    hidden_grad = lax.dot_general(scaled, down_rows, transposed, preferred_element_type=jnp.float32)
    grad_gate = (hidden_grad * up_pre * slope_val).astype(jnp.bfloat16)
    grad_up = (hidden_grad * activated).astype(jnp.bfloat16)
    back_gate = lax.dot_general(
        grad_gate, gate_cols, transposed, preferred_element_type=jnp.float32
    )
    back_up = lax.dot_general(grad_up, up_cols, transposed, preferred_element_type=jnp.float32)
    group_grad = (back_gate + back_up).astype(jnp.bfloat16)
    return (hidden, group_out, group_grad)


def split_half(stacked, upper_half):
    half_width = stacked.shape[-1] // 2
    lower_part = stacked[..., :half_width]
    upper_part = stacked[..., half_width:]
    kept_half = jnp.where(upper_half, upper_part, lower_part)
    sent_half = jnp.where(upper_half, lower_part, upper_part)
    return (kept_half, sent_half)


def layer(tokens, cotangent, expert_ids, gates, w_gate, w_up, w_down):
    highest = lax.Precision.HIGHEST
    tok_count, model_width = tokens.shape
    experts_here = lax.axis_size("eg")
    shards = lax.axis_size("es")
    capacity = tok_count // 24
    slot_count = experts_here * capacity
    window_ids = jnp.arange(experts_here, dtype=jnp.int32)
    named = expert_ids[:, :, None] == window_ids[None, None, :]
    present = jnp.any(named, axis=1).astype(jnp.float32)
    token_pos = jnp.arange(tok_count, dtype=jnp.int32)
    before = (token_pos[None, :] < token_pos[:, None]).astype(jnp.float32)
    prefix = jnp.dot(before, present, precision=highest)
    ranks = jnp.arange(capacity, dtype=jnp.float32)
    pick_block = present.T[:, None, :] * (prefix.T[:, None, :] == ranks[None, :, None])
    pick_token = pick_block.reshape(slot_count, tok_count)
    gate_te = jnp.sum(jnp.where(named, gates[:, :, None], 0.0), axis=1)
    slot_gate = jnp.sum(pick_block * gate_te.T[:, None, :], axis=2).reshape(slot_count)
    pick_narrow = pick_token.astype(jnp.bfloat16)
    slot_rows = jnp.dot(pick_narrow, tokens, preferred_element_type=jnp.float32).astype(
        jnp.bfloat16
    )
    slot_cot = jnp.dot(pick_narrow, cotangent, preferred_element_type=jnp.float32)
    slot_scaled = (slot_gate[:, None] * slot_cot).astype(jnp.bfloat16)

    tile_rows = 16
    payload = jnp.concatenate([slot_rows, slot_scaled], axis=1).reshape(
        experts_here, tile_rows, -1
    )
    arrived = lax.all_to_all(payload, "eg", 0, 0, tiled=True)
    copies = jnp.broadcast_to(arrived[None], (shards,) + arrived.shape).reshape(
        (shards * experts_here,) + arrived.shape[1:]
    )
    gathered = lax.all_to_all(copies, "es", 0, 0, tiled=True)
    gathered = gathered.reshape(shards * experts_here * capacity, 2 * model_width)
    inputs = gathered[:, :model_width]
    scaled = gathered[:, model_width:]
    hidden, group_out, group_grad = expert_rows(
        inputs, scaled, w_gate[0], w_up[0], w_down[0]
    )

    parts = jnp.concatenate([group_out, group_grad], axis=1).reshape(shards, slot_count, -1)
    parts = lax.all_to_all(parts, "es", 0, 0, tiled=True)
    summed = parts.astype(jnp.float32).sum(axis=0)
    summed = summed.astype(jnp.bfloat16).reshape(experts_here, tile_rows, -1)
    returned = lax.all_to_all(summed, "eg", 0, 0, tiled=True)
    returned = returned.reshape(slot_count, 2 * model_width).astype(jnp.float32)
    expert_out = returned[:, :model_width]
    grad_terms = returned[:, model_width:]

    weighted = slot_gate[:, None] * expert_out
    mixed_out = jnp.dot(pick_token.T, weighted, precision=highest).astype(jnp.bfloat16)
    slot_value = jnp.sum(slot_cot * expert_out, axis=1)
    value_te = jnp.sum(pick_block * slot_value.reshape(experts_here, capacity, 1), axis=1)
    gate_grad = jnp.sum(jnp.where(named, value_te.T[:, None, :], 0.0), axis=2)
    token_grad = jnp.dot(pick_token.T, grad_terms, precision=highest).astype(jnp.bfloat16)
    local_down = lax.dot_general(
        hidden,
        scaled,
        (((0,), (0,)), ((), ())),
        preferred_element_type=jnp.float32,
    ).astype(jnp.bfloat16)
    sections = lax.axis_size("pipe")
    section_pos = lax.axis_index("pipe")
    kept_half, sent_half = split_half(local_down, section_pos >= sections // 2)
    mirror = [(p, sections - 1 - p) for p in range(sections)]
    partner_part = lax.ppermute(sent_half, "pipe", mirror)
    partner_part = partner_part.astype(jnp.float32)
    down_grad = (kept_half.astype(jnp.float32) + partner_part).astype(jnp.bfloat16)[None]
    return (mixed_out, token_grad, gate_grad, down_grad)


def solution(mesh):
    experts = mesh.shape["expert"]
    split = Mesh(
        mesh.devices.reshape(mesh.shape["pipe"], experts // WS, WS), ("pipe", "eg", "es")
    )
    rows = P(("pipe", "eg", "es"), None)
    placed = (
        rows,
        rows,
        rows,
        rows,
        P("pipe", None, ("eg", "es")),
        P("pipe", None, ("eg", "es")),
        P("pipe", ("eg", "es"), None),
    )
    return jax.shard_map(
        layer,
        mesh=split,
        in_specs=placed,
        out_specs=(rows, rows, rows, P("pipe", ("eg", "es"), None)),
        check_vma=False,
    )
```

```python
import jax
import jax.numpy as jnp
from jax import lax
from jax.sharding import Mesh, PartitionSpec as P


WS = 4


def silu_parts(preact):
    sigmoid_val = jax.nn.sigmoid(preact)
    return (preact * sigmoid_val, sigmoid_val * (1.0 + preact * (1.0 - sigmoid_val)))


def expert_rows(inputs, scaled, gate_cols, up_cols, down_rows):
    transposed = (((1,), (1,)), ((), ()))
    gate_pre = jnp.dot(inputs, gate_cols, preferred_element_type=jnp.float32)
    up_pre = jnp.dot(inputs, up_cols, preferred_element_type=jnp.float32)
    activated, slope_val = silu_parts(gate_pre)
    hidden = (activated * up_pre).astype(jnp.bfloat16)
    group_out = jnp.dot(hidden, down_rows, preferred_element_type=jnp.float32).astype(jnp.bfloat16)
    hidden_grad = lax.dot_general(scaled, down_rows, transposed, preferred_element_type=jnp.float32)
    grad_gate = (hidden_grad * up_pre * slope_val).astype(jnp.bfloat16)
    grad_up = (hidden_grad * activated).astype(jnp.bfloat16)
    back_gate = lax.dot_general(
        grad_gate, gate_cols, transposed, preferred_element_type=jnp.float32
    )
    back_up = lax.dot_general(grad_up, up_cols, transposed, preferred_element_type=jnp.float32)
    group_grad = (back_gate + back_up).astype(jnp.bfloat16)
    return (hidden, group_out, group_grad)


def split_half(stacked, upper_half):
    half_width = stacked.shape[-1] // 2
    lower_part = stacked[..., :half_width]
    upper_part = stacked[..., half_width:]
    kept_half = jnp.where(upper_half, upper_part, lower_part)
    sent_half = jnp.where(upper_half, lower_part, upper_part)
    return (kept_half, sent_half)


def layer(tokens, cotangent, expert_ids, gates, w_gate, w_up, w_down):
    tok_count, model_width = tokens.shape
    experts_here = lax.axis_size("eg")
    shards = lax.axis_size("es")
    capacity = tok_count // 24
    slot_count = experts_here * capacity
    window_ids = jnp.arange(experts_here, dtype=jnp.int32)
    named = expert_ids[:, :, None] == window_ids[None, None, :]
    present = jnp.any(named, axis=1).astype(jnp.float32)
    token_pos = jnp.arange(tok_count, dtype=jnp.int32)
    before = (token_pos[None, :] < token_pos[:, None]).astype(jnp.float32)
    prefix = jnp.dot(before, present, preferred_element_type=jnp.float32)
    ranks = jnp.arange(capacity, dtype=jnp.float32)
    pick_block = present.T[:, None, :] * (prefix.T[:, None, :] == ranks[None, :, None])
    pick_token = pick_block.reshape(slot_count, tok_count)
    gate_te = jnp.sum(jnp.where(named, gates[:, :, None], 0.0), axis=1)
    slot_gate = jnp.sum(pick_block * gate_te.T[:, None, :], axis=2).reshape(slot_count)
    pick_narrow = pick_token.astype(jnp.bfloat16)
    slot_rows = jnp.dot(pick_narrow, tokens, preferred_element_type=jnp.float32).astype(
        jnp.bfloat16
    )
    slot_cot = jnp.dot(pick_narrow, cotangent, preferred_element_type=jnp.float32)
    slot_scaled = (slot_gate[:, None] * slot_cot).astype(jnp.bfloat16)

    tile_rows = 16
    payload = jnp.concatenate([slot_rows, slot_scaled], axis=1).reshape(
        experts_here, tile_rows, -1
    )
    arrived = lax.all_to_all(payload, "eg", 0, 0, tiled=True)
    copies = jnp.broadcast_to(arrived[None], (shards,) + arrived.shape).reshape(
        (shards * experts_here,) + arrived.shape[1:]
    )
    gathered = lax.all_to_all(copies, "es", 0, 0, tiled=True)
    gathered = gathered.reshape(shards * experts_here * capacity, 2 * model_width)
    inputs = gathered[:, :model_width]
    scaled = gathered[:, model_width:]
    hidden, group_out, group_grad = expert_rows(
        inputs, scaled, w_gate[0], w_up[0], w_down[0]
    )

    parts = jnp.concatenate([group_out, group_grad], axis=1).reshape(shards, slot_count, -1)
    parts = lax.all_to_all(parts, "es", 0, 0, tiled=True)
    summed = parts.astype(jnp.float32).sum(axis=0)
    summed = summed.astype(jnp.bfloat16).reshape(experts_here, tile_rows, -1)
    returned = lax.all_to_all(summed, "eg", 0, 0, tiled=True)
    returned = returned.reshape(slot_count, 2 * model_width).astype(jnp.float32)
    expert_out = returned[:, :model_width]
    grad_terms = returned[:, model_width:]

    weighted = slot_gate[:, None] * expert_out
    mixed_out = jnp.dot(pick_token.T, weighted, precision=lax.Precision.HIGH)
    mixed_out = mixed_out.astype(jnp.bfloat16)
    slot_value = jnp.sum(slot_cot * expert_out, axis=1)
    value_te = jnp.sum(pick_block * slot_value.reshape(experts_here, capacity, 1), axis=1)
    gate_grad = jnp.sum(jnp.where(named, value_te.T[:, None, :], 0.0), axis=2)
    token_grad = jnp.dot(pick_token.T, grad_terms, preferred_element_type=jnp.float32)
    token_grad = token_grad.astype(jnp.bfloat16)
    local_down = lax.dot_general(
        hidden,
        scaled,
        (((0,), (0,)), ((), ())),
        preferred_element_type=jnp.float32,
    ).astype(jnp.bfloat16)
    halves = lax.axis_size("zh")
    rings = lax.axis_size("yy")
    half_pos = lax.axis_index("zh")
    ring_pos = lax.axis_index("yy")
    kept_half, sent_half = split_half(local_down, half_pos >= halves // 2)
    around = lax.all_gather(sent_half, "yy", axis=0)
    reflected = lax.dynamic_index_in_dim(around, rings - 1 - ring_pos, 0, keepdims=False)
    across = lax.all_gather(reflected, "zh", axis=0)
    partner_part = lax.dynamic_index_in_dim(across, halves - 1 - half_pos, 0, keepdims=False)
    partner_part = partner_part.astype(jnp.float32)
    down_grad = (kept_half.astype(jnp.float32) + partner_part).astype(jnp.bfloat16)[None]
    return (mixed_out, token_grad, gate_grad, down_grad)


def solution(mesh):
    experts = mesh.shape["expert"]
    sections = mesh.shape["pipe"]
    split = Mesh(
        mesh.devices.reshape(2, sections // 2, experts // WS, WS), ("zh", "yy", "eg", "es")
    )
    rows = P(("zh", "yy", "eg", "es"), None)
    placed = (
        rows,
        rows,
        rows,
        rows,
        P(("zh", "yy"), None, ("eg", "es")),
        P(("zh", "yy"), None, ("eg", "es")),
        P(("zh", "yy"), ("eg", "es"), None),
    )
    return jax.shard_map(
        layer,
        mesh=split,
        in_specs=placed,
        out_specs=(rows, rows, rows, P(("zh", "yy"), ("eg", "es"), None)),
        check_vma=False,
    )
```

```python
import jax
import jax.numpy as jnp
from jax import lax
from jax.sharding import Mesh, PartitionSpec as P


WS = 4


def silu_parts(preact):
    sigmoid_val = jax.nn.sigmoid(preact)
    return (preact * sigmoid_val, sigmoid_val * (1.0 + preact * (1.0 - sigmoid_val)))


def expert_rows(inputs, scaled, gate_cols, up_cols, down_rows):
    transposed = (((1,), (1,)), ((), ()))
    gate_pre = jnp.dot(inputs, gate_cols, preferred_element_type=jnp.float32)
    up_pre = jnp.dot(inputs, up_cols, preferred_element_type=jnp.float32)
    activated, slope_val = silu_parts(gate_pre)
    hidden = (activated * up_pre).astype(jnp.bfloat16)
    group_out = jnp.dot(hidden, down_rows, preferred_element_type=jnp.float32).astype(jnp.bfloat16)
    hidden_grad = lax.dot_general(scaled, down_rows, transposed, preferred_element_type=jnp.float32)
    grad_gate = (hidden_grad * up_pre * slope_val).astype(jnp.bfloat16)
    grad_up = (hidden_grad * activated).astype(jnp.bfloat16)
    back_gate = lax.dot_general(
        grad_gate, gate_cols, transposed, preferred_element_type=jnp.float32
    )
    back_up = lax.dot_general(grad_up, up_cols, transposed, preferred_element_type=jnp.float32)
    group_grad = (back_gate + back_up).astype(jnp.bfloat16)
    return (hidden, group_out, group_grad)


def split_half(stacked, upper_half):
    half_width = stacked.shape[-1] // 2
    lower_part = stacked[..., :half_width]
    upper_part = stacked[..., half_width:]
    kept_half = jnp.where(upper_half, upper_part, lower_part)
    sent_half = jnp.where(upper_half, lower_part, upper_part)
    return (kept_half, sent_half)


def layer(tokens, cotangent, expert_ids, gates, w_gate, w_up, w_down):
    tok_count, model_width = tokens.shape
    experts_here = lax.axis_size("eg")
    shards = lax.axis_size("es")
    capacity = tok_count // 24
    slot_count = experts_here * capacity
    window_ids = jnp.arange(experts_here, dtype=jnp.int32)
    named = expert_ids[:, :, None] == window_ids[None, None, :]
    present = jnp.any(named, axis=1).astype(jnp.float32)
    token_pos = jnp.arange(tok_count, dtype=jnp.int32)
    before = (token_pos[None, :] < token_pos[:, None]).astype(jnp.float32)
    prefix = jnp.dot(before, present, preferred_element_type=jnp.float32)
    ranks = jnp.arange(capacity, dtype=jnp.float32)
    pick_block = present.T[:, None, :] * (prefix.T[:, None, :] == ranks[None, :, None])
    pick_token = pick_block.reshape(slot_count, tok_count)
    gate_te = jnp.sum(jnp.where(named, gates[:, :, None], 0.0), axis=1)
    slot_gate = jnp.sum(pick_block * gate_te.T[:, None, :], axis=2).reshape(slot_count)
    pick_narrow = pick_token.astype(jnp.bfloat16)
    slot_rows = jnp.dot(pick_narrow, tokens, preferred_element_type=jnp.float32).astype(
        jnp.bfloat16
    )
    slot_cot = jnp.dot(pick_narrow, cotangent, preferred_element_type=jnp.float32)
    slot_scaled = (slot_gate[:, None] * slot_cot).astype(jnp.bfloat16)

    tile_rows = 16
    payload = jnp.concatenate([slot_rows, slot_scaled], axis=1).reshape(
        experts_here, tile_rows, -1
    )
    arrived = lax.all_to_all(payload, "eg", 0, 0, tiled=True)
    copies = jnp.broadcast_to(arrived[None], (shards,) + arrived.shape).reshape(
        (shards * experts_here,) + arrived.shape[1:]
    )
    gathered = lax.all_to_all(copies, "es", 0, 0, tiled=True)
    gathered = gathered.reshape(shards * experts_here * capacity, 2 * model_width)
    inputs = gathered[:, :model_width]
    scaled = gathered[:, model_width:]
    hidden, group_out, group_grad = expert_rows(
        inputs, scaled, w_gate[0], w_up[0], w_down[0]
    )

    parts = jnp.concatenate([group_out, group_grad], axis=1).reshape(shards, slot_count, -1)
    parts = lax.all_to_all(parts, "es", 0, 0, tiled=True)
    summed = parts.astype(jnp.float32).sum(axis=0)
    summed = summed.astype(jnp.bfloat16).reshape(experts_here, tile_rows, -1)
    returned = lax.all_to_all(summed, "eg", 0, 0, tiled=True)
    returned = returned.reshape(slot_count, 2 * model_width).astype(jnp.float32)
    expert_out = returned[:, :model_width]
    grad_terms = returned[:, model_width:]

    weighted = slot_gate[:, None] * expert_out
    mixed_out = jnp.dot(pick_token.T, weighted, precision=lax.Precision.HIGH)
    mixed_out = mixed_out.astype(jnp.bfloat16)
    slot_value = jnp.sum(slot_cot * expert_out, axis=1)
    value_te = jnp.sum(pick_block * slot_value.reshape(experts_here, capacity, 1), axis=1)
    gate_grad = jnp.sum(jnp.where(named, value_te.T[:, None, :], 0.0), axis=2)
    token_grad = jnp.dot(pick_token.T, grad_terms, preferred_element_type=jnp.float32)
    token_grad = token_grad.astype(jnp.bfloat16)
    local_down = lax.dot_general(
        hidden,
        scaled,
        (((0,), (0,)), ((), ())),
        preferred_element_type=jnp.float32,
    ).astype(jnp.bfloat16)
    sections = lax.axis_size("pipe")
    section_pos = lax.axis_index("pipe")
    kept_half, sent_half = split_half(local_down, section_pos >= sections // 2)
    mirror = [(p, sections - 1 - p) for p in range(sections)]
    partner_part = lax.ppermute(sent_half, "pipe", mirror)
    partner_part = partner_part.astype(jnp.float32)
    down_grad = (kept_half.astype(jnp.float32) + partner_part).astype(jnp.bfloat16)[None]
    return (mixed_out, token_grad, gate_grad, down_grad)


def solution(mesh):
    experts = mesh.shape["expert"]
    split = Mesh(
        mesh.devices.reshape(mesh.shape["pipe"], experts // WS, WS), ("pipe", "eg", "es")
    )
    rows = P(("pipe", "eg", "es"), None)
    placed = (
        rows,
        rows,
        rows,
        rows,
        P("pipe", None, ("eg", "es")),
        P("pipe", None, ("eg", "es")),
        P("pipe", ("eg", "es"), None),
    )
    return jax.shard_map(
        layer,
        mesh=split,
        in_specs=placed,
        out_specs=(rows, rows, rows, P("pipe", ("eg", "es"), None)),
        check_vma=False,
    )
```

```python
import jax
import jax.numpy as jnp
from jax import lax
from jax.sharding import Mesh, PartitionSpec as P


WS = 4


def silu_parts(preact):
    sigmoid_val = jax.nn.sigmoid(preact)
    return (preact * sigmoid_val, sigmoid_val * (1.0 + preact * (1.0 - sigmoid_val)))


def expert_rows(inputs, scaled, gate_cols, up_cols, down_rows):
    transposed = (((1,), (1,)), ((), ()))
    gate_pre = jnp.dot(inputs, gate_cols, preferred_element_type=jnp.float32)
    up_pre = jnp.dot(inputs, up_cols, preferred_element_type=jnp.float32)
    activated, slope_val = silu_parts(gate_pre)
    hidden = (activated * up_pre).astype(jnp.bfloat16)
    group_out = jnp.dot(hidden, down_rows, preferred_element_type=jnp.float32).astype(jnp.bfloat16)
    hidden_grad = lax.dot_general(scaled, down_rows, transposed, preferred_element_type=jnp.float32)
    grad_gate = (hidden_grad * up_pre * slope_val).astype(jnp.bfloat16)
    grad_up = (hidden_grad * activated).astype(jnp.bfloat16)
    back_gate = lax.dot_general(
        grad_gate, gate_cols, transposed, preferred_element_type=jnp.float32
    )
    back_up = lax.dot_general(grad_up, up_cols, transposed, preferred_element_type=jnp.float32)
    group_grad = (back_gate + back_up).astype(jnp.bfloat16)
    return (hidden, group_out, group_grad)


def split_half(stacked, upper_half):
    half_width = stacked.shape[-1] // 2
    lower_part = stacked[..., :half_width]
    upper_part = stacked[..., half_width:]
    kept_half = jnp.where(upper_half, upper_part, lower_part)
    sent_half = jnp.where(upper_half, lower_part, upper_part)
    return (kept_half, sent_half)


def layer(tokens, cotangent, expert_ids, gates, w_gate, w_up, w_down):
    tok_count, model_width = tokens.shape
    experts_here = lax.axis_size("eg")
    shards = lax.axis_size("xs") * lax.axis_size("core")
    capacity = tok_count // 24
    slot_count = experts_here * capacity
    window_ids = jnp.arange(experts_here, dtype=jnp.int32)
    named = expert_ids[:, :, None] == window_ids[None, None, :]
    present = jnp.any(named, axis=1).astype(jnp.float32)
    token_pos = jnp.arange(tok_count, dtype=jnp.int32)
    before = (token_pos[None, :] < token_pos[:, None]).astype(jnp.float32)
    prefix = jnp.dot(before, present, preferred_element_type=jnp.float32)
    ranks = jnp.arange(capacity, dtype=jnp.float32)
    pick_block = present.T[:, None, :] * (prefix.T[:, None, :] == ranks[None, :, None])
    pick_token = pick_block.reshape(slot_count, tok_count)
    gate_te = jnp.sum(jnp.where(named, gates[:, :, None], 0.0), axis=1)
    slot_gate = jnp.sum(pick_block * gate_te.T[:, None, :], axis=2).reshape(slot_count)
    pick_narrow = pick_token.astype(jnp.bfloat16)
    slot_rows = jnp.dot(pick_narrow, tokens, preferred_element_type=jnp.float32).astype(
        jnp.bfloat16
    )
    slot_cot = jnp.dot(pick_narrow, cotangent, preferred_element_type=jnp.float32)
    slot_scaled = (slot_gate[:, None] * slot_cot).astype(jnp.bfloat16)

    tile_rows = 16
    payload = jnp.concatenate([slot_rows, slot_scaled], axis=1).reshape(
        experts_here, tile_rows, -1
    )
    arrived = lax.all_to_all(payload, "eg", 0, 0, tiled=True)
    pair = jnp.broadcast_to(arrived[None], (2,) + arrived.shape).reshape(
        (2 * experts_here,) + arrived.shape[1:]
    )
    pair = lax.all_to_all(pair, "xs", 0, 0, tiled=True)
    copies = jnp.broadcast_to(pair[None], (2,) + pair.shape).reshape(
        (shards * experts_here,) + arrived.shape[1:]
    )
    gathered = lax.all_to_all(copies, "core", 0, 0, tiled=True)
    gathered = gathered.reshape(shards * experts_here * capacity, 2 * model_width)
    inputs = gathered[:, :model_width]
    scaled = gathered[:, model_width:]
    hidden, group_out, group_grad = expert_rows(
        inputs, scaled, w_gate[0], w_up[0], w_down[0]
    )

    parts = jnp.concatenate([group_out, group_grad], axis=1).reshape(2, 2 * slot_count, -1)
    parts = lax.all_to_all(parts, "core", 0, 0, tiled=True)
    on_chip = parts.astype(jnp.float32).sum(axis=0).astype(jnp.bfloat16)
    on_chip = on_chip.reshape(2, slot_count, -1)
    across = lax.all_to_all(on_chip, "xs", 0, 0, tiled=True)
    summed = across.astype(jnp.float32).sum(axis=0)
    summed = summed.astype(jnp.bfloat16).reshape(experts_here, tile_rows, -1)
    returned = lax.all_to_all(summed, "eg", 0, 0, tiled=True)
    returned = returned.reshape(slot_count, 2 * model_width).astype(jnp.float32)
    expert_out = returned[:, :model_width]
    grad_terms = returned[:, model_width:]

    weighted = slot_gate[:, None] * expert_out
    mixed_out = jnp.dot(pick_token.T, weighted, precision=lax.Precision.HIGH)
    mixed_out = mixed_out.astype(jnp.bfloat16)
    slot_value = jnp.sum(slot_cot * expert_out, axis=1)
    value_te = jnp.sum(pick_block * slot_value.reshape(experts_here, capacity, 1), axis=1)
    gate_grad = jnp.sum(jnp.where(named, value_te.T[:, None, :], 0.0), axis=2)
    token_grad = jnp.dot(pick_token.T, grad_terms, preferred_element_type=jnp.float32)
    token_grad = token_grad.astype(jnp.bfloat16)
    local_down = lax.dot_general(
        hidden,
        scaled,
        (((0,), (0,)), ((), ())),
        preferred_element_type=jnp.float32,
    ).astype(jnp.bfloat16)
    sections = lax.axis_size("pipe")
    section_pos = lax.axis_index("pipe")
    kept_half, sent_half = split_half(local_down, section_pos >= sections // 2)
    mirror = [(p, sections - 1 - p) for p in range(sections)]
    partner_part = lax.ppermute(sent_half, "pipe", mirror)
    partner_part = partner_part.astype(jnp.float32)
    down_grad = (kept_half.astype(jnp.float32) + partner_part).astype(jnp.bfloat16)[None]
    return (mixed_out, token_grad, gate_grad, down_grad)


def solution(mesh):
    experts = mesh.shape["expert"]
    split = Mesh(
        mesh.devices.reshape(mesh.shape["pipe"], experts // WS, 2, WS // 2),
        ("pipe", "eg", "xs", "core"),
    )
    shard = ("eg", "xs", "core")
    rows = P(("pipe",) + shard, None)
    placed = (
        rows,
        rows,
        rows,
        rows,
        P("pipe", None, shard),
        P("pipe", None, shard),
        P("pipe", shard, None),
    )
    return jax.shard_map(
        layer,
        mesh=split,
        in_specs=placed,
        out_specs=(rows, rows, rows, P("pipe", shard, None)),
        check_vma=False,
    )
```

```python
import jax
import jax.numpy as jnp
from jax import lax
from jax.sharding import Mesh, PartitionSpec as P


WS = 4


def silu_parts(preact):
    sigmoid_val = jax.nn.sigmoid(preact)
    return (preact * sigmoid_val, sigmoid_val * (1.0 + preact * (1.0 - sigmoid_val)))


def expert_rows(inputs, scaled, gate_cols, up_cols, down_rows):
    transposed = (((1,), (1,)), ((), ()))
    gate_pre = jnp.dot(inputs, gate_cols, preferred_element_type=jnp.float32)
    up_pre = jnp.dot(inputs, up_cols, preferred_element_type=jnp.float32)
    activated, slope_val = silu_parts(gate_pre)
    hidden = (activated * up_pre).astype(jnp.bfloat16)
    group_out = jnp.dot(hidden, down_rows, preferred_element_type=jnp.float32).astype(jnp.bfloat16)
    hidden_grad = lax.dot_general(scaled, down_rows, transposed, preferred_element_type=jnp.float32)
    grad_gate = (hidden_grad * up_pre * slope_val).astype(jnp.bfloat16)
    grad_up = (hidden_grad * activated).astype(jnp.bfloat16)
    back_gate = lax.dot_general(
        grad_gate, gate_cols, transposed, preferred_element_type=jnp.float32
    )
    back_up = lax.dot_general(grad_up, up_cols, transposed, preferred_element_type=jnp.float32)
    group_grad = (back_gate + back_up).astype(jnp.bfloat16)
    return (hidden, group_out, group_grad)


def split_half(stacked, upper_half):
    half_width = stacked.shape[-1] // 2
    lower_part = stacked[..., :half_width]
    upper_part = stacked[..., half_width:]
    kept_half = jnp.where(upper_half, upper_part, lower_part)
    sent_half = jnp.where(upper_half, lower_part, upper_part)
    return (kept_half, sent_half)


def layer(tokens, cotangent, expert_ids, gates, w_gate, w_up, w_down):
    tok_count, model_width = tokens.shape
    experts_here = lax.axis_size("eg")
    shards = lax.axis_size("xs") * lax.axis_size("core")
    capacity = tok_count // 24
    slot_count = experts_here * capacity
    window_ids = jnp.arange(experts_here, dtype=jnp.int32)
    named = expert_ids[:, :, None] == window_ids[None, None, :]
    present = jnp.any(named, axis=1).astype(jnp.float32)
    token_pos = jnp.arange(tok_count, dtype=jnp.int32)
    before = (token_pos[None, :] < token_pos[:, None]).astype(jnp.float32)
    prefix = jnp.dot(before, present, preferred_element_type=jnp.float32)
    ranks = jnp.arange(capacity, dtype=jnp.float32)
    pick_block = present.T[:, None, :] * (prefix.T[:, None, :] == ranks[None, :, None])
    pick_token = pick_block.reshape(slot_count, tok_count)
    gate_te = jnp.sum(jnp.where(named, gates[:, :, None], 0.0), axis=1)
    slot_gate = jnp.sum(pick_block * gate_te.T[:, None, :], axis=2).reshape(slot_count)
    pick_narrow = pick_token.astype(jnp.bfloat16)
    slot_rows = jnp.dot(pick_narrow, tokens, preferred_element_type=jnp.float32).astype(
        jnp.bfloat16
    )
    slot_cot = jnp.dot(pick_narrow, cotangent, preferred_element_type=jnp.float32)
    slot_scaled = (slot_gate[:, None] * slot_cot).astype(jnp.bfloat16)

    tile_rows = 16
    payload = jnp.concatenate([slot_rows, slot_scaled], axis=1).reshape(
        experts_here, tile_rows, -1
    )
    arrived = lax.all_to_all(payload, "eg", 0, 0, tiled=True)
    pair = jnp.broadcast_to(arrived[None], (2,) + arrived.shape).reshape(
        (2 * experts_here,) + arrived.shape[1:]
    )
    pair = lax.all_to_all(pair, "xs", 0, 0, tiled=True)
    swap = [(0, 1), (1, 0)]
    gathered = jnp.concatenate([pair, lax.ppermute(pair, "core", swap)])
    gathered = gathered.reshape(shards * experts_here * capacity, 2 * model_width)
    inputs = gathered[:, :model_width]
    scaled = gathered[:, model_width:]
    hidden, group_out, group_grad = expert_rows(
        inputs, scaled, w_gate[0], w_up[0], w_down[0]
    )

    parts = jnp.concatenate([group_out, group_grad], axis=1).reshape(2, 2 * slot_count, -1)
    other = lax.ppermute(parts[1], "core", swap)
    on_chip = (parts[0].astype(jnp.float32) + other.astype(jnp.float32)).astype(jnp.bfloat16)
    on_chip = on_chip.reshape(2, slot_count, -1)
    across = lax.all_to_all(on_chip, "xs", 0, 0, tiled=True)
    summed = across.astype(jnp.float32).sum(axis=0)
    summed = summed.astype(jnp.bfloat16).reshape(experts_here, tile_rows, -1)
    returned = lax.all_to_all(summed, "eg", 0, 0, tiled=True)
    returned = returned.reshape(slot_count, 2 * model_width).astype(jnp.float32)
    expert_out = returned[:, :model_width]
    grad_terms = returned[:, model_width:]

    weighted = slot_gate[:, None] * expert_out
    mixed_out = jnp.dot(pick_token.T, weighted, precision=lax.Precision.HIGH)
    mixed_out = mixed_out.astype(jnp.bfloat16)
    slot_value = jnp.sum(slot_cot * expert_out, axis=1)
    value_te = jnp.sum(pick_block * slot_value.reshape(experts_here, capacity, 1), axis=1)
    gate_grad = jnp.sum(jnp.where(named, value_te.T[:, None, :], 0.0), axis=2)
    token_grad = jnp.dot(pick_token.T, grad_terms, preferred_element_type=jnp.float32)
    token_grad = token_grad.astype(jnp.bfloat16)
    local_down = lax.dot_general(
        hidden,
        scaled,
        (((0,), (0,)), ((), ())),
        preferred_element_type=jnp.float32,
    ).astype(jnp.bfloat16)
    sections = lax.axis_size("pipe")
    section_pos = lax.axis_index("pipe")
    kept_half, sent_half = split_half(local_down, section_pos >= sections // 2)
    mirror = [(p, sections - 1 - p) for p in range(sections)]
    partner_part = lax.ppermute(sent_half, "pipe", mirror)
    partner_part = partner_part.astype(jnp.float32)
    down_grad = (kept_half.astype(jnp.float32) + partner_part).astype(jnp.bfloat16)[None]
    return (mixed_out, token_grad, gate_grad, down_grad)


def solution(mesh):
    experts = mesh.shape["expert"]
    split = Mesh(
        mesh.devices.reshape(mesh.shape["pipe"], experts // WS, 2, WS // 2),
        ("pipe", "eg", "xs", "core"),
    )
    shard = ("eg", "xs", "core")
    rows = P(("pipe",) + shard, None)
    placed = (
        rows,
        rows,
        rows,
        rows,
        P("pipe", None, shard),
        P("pipe", None, shard),
        P("pipe", shard, None),
    )
    return jax.shard_map(
        layer,
        mesh=split,
        in_specs=placed,
        out_specs=(rows, rows, rows, P("pipe", shard, None)),
        check_vma=False,
    )
```

```python
import jax
import jax.numpy as jnp
from jax import lax
from jax.sharding import Mesh, PartitionSpec as P


WS = 4


def silu_parts(preact):
    sigmoid_val = jax.nn.sigmoid(preact)
    return (preact * sigmoid_val, sigmoid_val * (1.0 + preact * (1.0 - sigmoid_val)))


def expert_rows(inputs, scaled, gate_cols, up_cols, down_rows):
    transposed = (((1,), (1,)), ((), ()))
    gate_pre = jnp.dot(inputs, gate_cols, preferred_element_type=jnp.float32)
    up_pre = jnp.dot(inputs, up_cols, preferred_element_type=jnp.float32)
    activated, slope_val = silu_parts(gate_pre)
    hidden = (activated * up_pre).astype(jnp.bfloat16)
    group_out = jnp.dot(hidden, down_rows, preferred_element_type=jnp.float32).astype(jnp.bfloat16)
    hidden_grad = lax.dot_general(scaled, down_rows, transposed, preferred_element_type=jnp.float32)
    grad_gate = (hidden_grad * up_pre * slope_val).astype(jnp.bfloat16)
    grad_up = (hidden_grad * activated).astype(jnp.bfloat16)
    back_gate = lax.dot_general(
        grad_gate, gate_cols, transposed, preferred_element_type=jnp.float32
    )
    back_up = lax.dot_general(grad_up, up_cols, transposed, preferred_element_type=jnp.float32)
    group_grad = (back_gate + back_up).astype(jnp.bfloat16)
    return (hidden, group_out, group_grad)


def split_half(stacked, upper_half):
    half_width = stacked.shape[-1] // 2
    lower_part = stacked[..., :half_width]
    upper_part = stacked[..., half_width:]
    kept_half = jnp.where(upper_half, upper_part, lower_part)
    sent_half = jnp.where(upper_half, lower_part, upper_part)
    return (kept_half, sent_half)


def layer(tokens, cotangent, expert_ids, gates, w_gate, w_up, w_down):
    tok_count, model_width = tokens.shape
    experts_here = lax.axis_size("eg")
    shards = lax.axis_size("xs") * lax.axis_size("core")
    capacity = tok_count // 24
    slot_count = experts_here * capacity
    window_ids = jnp.arange(experts_here, dtype=jnp.int32)
    named = expert_ids[:, :, None] == window_ids[None, None, :]
    present = jnp.any(named, axis=1).astype(jnp.float32)
    token_pos = jnp.arange(tok_count, dtype=jnp.int32)
    before = (token_pos[None, :] < token_pos[:, None]).astype(jnp.float32)
    prefix = jnp.dot(before, present, preferred_element_type=jnp.float32)
    ranks = jnp.arange(capacity, dtype=jnp.float32)
    pick_block = present.T[:, None, :] * (prefix.T[:, None, :] == ranks[None, :, None])
    pick_token = pick_block.reshape(slot_count, tok_count)
    gate_te = jnp.sum(jnp.where(named, gates[:, :, None], 0.0), axis=1)
    slot_gate = jnp.sum(pick_block * gate_te.T[:, None, :], axis=2).reshape(slot_count)
    pick_narrow = pick_token.astype(jnp.bfloat16)
    slot_rows = jnp.dot(pick_narrow, tokens, preferred_element_type=jnp.float32).astype(
        jnp.bfloat16
    )
    slot_cot = jnp.dot(pick_narrow, cotangent, preferred_element_type=jnp.float32)
    slot_scaled = (slot_gate[:, None] * slot_cot).astype(jnp.bfloat16)

    tile_rows = 16
    payload = jnp.concatenate([slot_rows, slot_scaled], axis=1).reshape(
        experts_here, tile_rows, -1
    )
    arrived = lax.all_to_all(payload, "eg", 0, 0, tiled=True)
    swap = [(0, 1), (1, 0)]
    pair = jnp.concatenate([arrived, lax.ppermute(arrived, "xs", swap)])
    gathered = jnp.concatenate([pair, lax.ppermute(pair, "core", swap)])
    gathered = gathered.reshape(shards * experts_here * capacity, 2 * model_width)
    inputs = gathered[:, :model_width]
    scaled = gathered[:, model_width:]
    hidden, group_out, group_grad = expert_rows(
        inputs, scaled, w_gate[0], w_up[0], w_down[0]
    )

    parts = jnp.concatenate([group_out, group_grad], axis=1).reshape(2, 2 * slot_count, -1)
    other = lax.ppermute(parts[1], "core", swap)
    on_chip = (parts[0].astype(jnp.float32) + other.astype(jnp.float32)).astype(jnp.bfloat16)
    on_chip = on_chip.reshape(2, slot_count, -1)
    across = lax.ppermute(on_chip[1], "xs", swap)
    summed = on_chip[0].astype(jnp.float32) + across.astype(jnp.float32)
    summed = summed.astype(jnp.bfloat16).reshape(experts_here, tile_rows, -1)
    returned = lax.all_to_all(summed, "eg", 0, 0, tiled=True)
    returned = returned.reshape(slot_count, 2 * model_width).astype(jnp.float32)
    expert_out = returned[:, :model_width]
    grad_terms = returned[:, model_width:]

    weighted = slot_gate[:, None] * expert_out
    mixed_out = jnp.dot(pick_token.T, weighted, precision=lax.Precision.HIGH)
    mixed_out = mixed_out.astype(jnp.bfloat16)
    slot_value = jnp.sum(slot_cot * expert_out, axis=1)
    value_te = jnp.sum(pick_block * slot_value.reshape(experts_here, capacity, 1), axis=1)
    gate_grad = jnp.sum(jnp.where(named, value_te.T[:, None, :], 0.0), axis=2)
    token_grad = jnp.dot(pick_token.T, grad_terms, preferred_element_type=jnp.float32)
    token_grad = token_grad.astype(jnp.bfloat16)
    local_down = lax.dot_general(
        hidden,
        scaled,
        (((0,), (0,)), ((), ())),
        preferred_element_type=jnp.float32,
    ).astype(jnp.bfloat16)
    sections = lax.axis_size("pipe")
    section_pos = lax.axis_index("pipe")
    kept_half, sent_half = split_half(local_down, section_pos >= sections // 2)
    mirror = [(p, sections - 1 - p) for p in range(sections)]
    partner_part = lax.ppermute(sent_half, "pipe", mirror)
    partner_part = partner_part.astype(jnp.float32)
    down_grad = (kept_half.astype(jnp.float32) + partner_part).astype(jnp.bfloat16)[None]
    return (mixed_out, token_grad, gate_grad, down_grad)


def solution(mesh):
    experts = mesh.shape["expert"]
    split = Mesh(
        mesh.devices.reshape(mesh.shape["pipe"], experts // WS, 2, WS // 2),
        ("pipe", "eg", "xs", "core"),
    )
    shard = ("eg", "xs", "core")
    rows = P(("pipe",) + shard, None)
    placed = (
        rows,
        rows,
        rows,
        rows,
        P("pipe", None, shard),
        P("pipe", None, shard),
        P("pipe", shard, None),
    )
    return jax.shard_map(
        layer,
        mesh=split,
        in_specs=placed,
        out_specs=(rows, rows, rows, P("pipe", shard, None)),
        check_vma=False,
    )
```

```python
import jax
import jax.numpy as jnp
from jax import lax
from jax.sharding import Mesh, PartitionSpec as P


WS = 4


def silu_parts(preact):
    sigmoid_val = jax.nn.sigmoid(preact)
    return (preact * sigmoid_val, sigmoid_val * (1.0 + preact * (1.0 - sigmoid_val)))


def expert_rows(inputs, scaled, gate_cols, up_cols, down_rows):
    transposed = (((1,), (1,)), ((), ()))
    gate_pre = jnp.dot(inputs, gate_cols, preferred_element_type=jnp.float32)
    up_pre = jnp.dot(inputs, up_cols, preferred_element_type=jnp.float32)
    activated, slope_val = silu_parts(gate_pre)
    hidden = (activated * up_pre).astype(jnp.bfloat16)
    group_out = jnp.dot(hidden, down_rows, preferred_element_type=jnp.float32).astype(jnp.bfloat16)
    hidden_grad = lax.dot_general(scaled, down_rows, transposed, preferred_element_type=jnp.float32)
    grad_gate = (hidden_grad * up_pre * slope_val).astype(jnp.bfloat16)
    grad_up = (hidden_grad * activated).astype(jnp.bfloat16)
    back_gate = lax.dot_general(
        grad_gate, gate_cols, transposed, preferred_element_type=jnp.float32
    )
    back_up = lax.dot_general(grad_up, up_cols, transposed, preferred_element_type=jnp.float32)
    group_grad = (back_gate + back_up).astype(jnp.bfloat16)
    return (hidden, group_out, group_grad)


def split_half(stacked, upper_half):
    half_width = stacked.shape[-1] // 2
    lower_part = stacked[..., :half_width]
    upper_part = stacked[..., half_width:]
    kept_half = jnp.where(upper_half, upper_part, lower_part)
    sent_half = jnp.where(upper_half, lower_part, upper_part)
    return (kept_half, sent_half)


def layer(tokens, cotangent, expert_ids, gates, w_gate, w_up, w_down):
    tok_count, model_width = tokens.shape
    experts_here = lax.axis_size("eg")
    shards = lax.axis_size("xs") * lax.axis_size("core")
    capacity = tok_count // 24
    slot_count = experts_here * capacity
    window_ids = jnp.arange(experts_here, dtype=jnp.int32)
    named = expert_ids[:, :, None] == window_ids[None, None, :]
    present = jnp.any(named, axis=1).astype(jnp.float32)
    token_pos = jnp.arange(tok_count, dtype=jnp.int32)
    before = (token_pos[None, :] < token_pos[:, None]).astype(jnp.float32)
    prefix = jnp.dot(before, present, preferred_element_type=jnp.float32)
    ranks = jnp.arange(capacity, dtype=jnp.float32)
    pick_block = present.T[:, None, :] * (prefix.T[:, None, :] == ranks[None, :, None])
    pick_token = pick_block.reshape(slot_count, tok_count)
    gate_te = jnp.sum(jnp.where(named, gates[:, :, None], 0.0), axis=1)
    slot_gate = jnp.sum(pick_block * gate_te.T[:, None, :], axis=2).reshape(slot_count)
    pick_narrow = pick_token.astype(jnp.bfloat16)
    slot_rows = jnp.dot(pick_narrow, tokens, preferred_element_type=jnp.float32).astype(
        jnp.bfloat16
    )
    slot_cot = jnp.dot(pick_narrow, cotangent, preferred_element_type=jnp.float32)
    slot_scaled = (slot_gate[:, None] * slot_cot).astype(jnp.bfloat16)

    tile_rows = 16
    payload = jnp.concatenate([slot_rows, slot_scaled], axis=1).reshape(
        experts_here, tile_rows, -1
    )
    arrived = lax.all_to_all(payload, "eg", 0, 0, tiled=True)
    swap = [(0, 1), (1, 0)]
    partner = lax.ppermute(arrived, "xs", swap)
    beside = lax.ppermute(arrived, "core", swap)
    gathered = jnp.concatenate([arrived, partner, beside, lax.ppermute(partner, "core", swap)])
    gathered = gathered.reshape(shards * experts_here * capacity, 2 * model_width)
    inputs = gathered[:, :model_width]
    scaled = gathered[:, model_width:]
    hidden, group_out, group_grad = expert_rows(
        inputs, scaled, w_gate[0], w_up[0], w_down[0]
    )

    parts = jnp.concatenate([group_out, group_grad], axis=1).reshape(2, 2 * slot_count, -1)
    other = lax.ppermute(parts[1], "core", swap)
    on_chip = (parts[0].astype(jnp.float32) + other.astype(jnp.float32)).astype(jnp.bfloat16)
    on_chip = on_chip.reshape(2, slot_count, -1)
    across = lax.ppermute(on_chip[1], "xs", swap)
    summed = on_chip[0].astype(jnp.float32) + across.astype(jnp.float32)
    summed = summed.astype(jnp.bfloat16).reshape(experts_here, tile_rows, -1)
    returned = lax.all_to_all(summed, "eg", 0, 0, tiled=True)
    returned = returned.reshape(slot_count, 2 * model_width).astype(jnp.float32)
    expert_out = returned[:, :model_width]
    grad_terms = returned[:, model_width:]

    weighted = slot_gate[:, None] * expert_out
    mixed_out = jnp.dot(pick_token.T, weighted, precision=lax.Precision.HIGH)
    mixed_out = mixed_out.astype(jnp.bfloat16)
    slot_value = jnp.sum(slot_cot * expert_out, axis=1)
    value_te = jnp.sum(pick_block * slot_value.reshape(experts_here, capacity, 1), axis=1)
    gate_grad = jnp.sum(jnp.where(named, value_te.T[:, None, :], 0.0), axis=2)
    token_grad = jnp.dot(pick_token.T, grad_terms, preferred_element_type=jnp.float32)
    token_grad = token_grad.astype(jnp.bfloat16)
    local_down = lax.dot_general(
        hidden,
        scaled,
        (((0,), (0,)), ((), ())),
        preferred_element_type=jnp.float32,
    ).astype(jnp.bfloat16)
    sections = lax.axis_size("pipe")
    section_pos = lax.axis_index("pipe")
    kept_half, sent_half = split_half(local_down, section_pos >= sections // 2)
    mirror = [(p, sections - 1 - p) for p in range(sections)]
    partner_part = lax.ppermute(sent_half, "pipe", mirror)
    partner_part = partner_part.astype(jnp.float32)
    down_grad = (kept_half.astype(jnp.float32) + partner_part).astype(jnp.bfloat16)[None]
    return (mixed_out, token_grad, gate_grad, down_grad)


def solution(mesh):
    experts = mesh.shape["expert"]
    split = Mesh(
        mesh.devices.reshape(mesh.shape["pipe"], experts // WS, 2, WS // 2),
        ("pipe", "eg", "xs", "core"),
    )
    shard = ("eg", "xs", "core")
    rows = P(("pipe",) + shard, None)
    placed = (
        rows,
        rows,
        rows,
        rows,
        P("pipe", None, shard),
        P("pipe", None, shard),
        P("pipe", shard, None),
    )
    return jax.shard_map(
        layer,
        mesh=split,
        in_specs=placed,
        out_specs=(rows, rows, rows, P("pipe", shard, None)),
        check_vma=False,
    )
```
